512 devices in a mesh: gx: 32 (over z_hi, x, core), gy: 16 (over y, z_lo).
Axes of the slice: x: 4, y: 4, z: 16 (z_hi: 4, z_lo: 4; z = z_hi * 4 + z_lo), core: 2. Of those that a mesh axis runs over, the one named last changes fastest.
Arguments:
- orbitals: float32 [32, 64, 128, 512], P(None, 'gx', 'gy'), may hold values from -60 to 60
- potential: float32 [64, 128, 512], P('gx', 'gy'), may hold values from 0.2 to 2
- sign_bits: int32 [64, 128, 512], P('gx', 'gy'), may hold values from 0 to 1
- sampled_rows: int32 [32, 16, 8192], P('gx', 'gy'), may hold values from 0 to 8191, each once within a row
Outputs:
- rotated: float32 [32, 64, 128, 512], P(None, 'gx', 'gy')
- sketches: float32 [2, 32, 4096], P(None, None, ('gx', 'gy'))
- projected: float32 [32, 32], replicated
The draws below stay inside these ranges and needn't reach their ends.
Inputs may be any that keep to these rules, and one draw needn't show every extreme that they name: Each block's row of sampled_rows holds every one of its 8192 cell numbers once.
All inputs are finite; a program needn't handle non-finite values.
Results may differ from the reference program's by a relative error of at most 0.00026.
Values sent between devices are 32-bit elements; how exact they have to be, the bound alone decides.
No kernel may reach another device: no remote copies, remote signals or barrier semaphores. Data moves between devices by JAX's collectives and lax.ppermute only.
A program may use at most 64 MiB of HBM per device.

```python
import math
import jax
import jax.numpy as jnp
from jax import lax

NORB = 32
M = 4096
NZ = 512
CX = 2
CY = 8
CELLS_DEV = 8192
NX = 64
NY = 128
N_GX = 32
N_GY = 16


def draw_orbitals(key, part):
    key_orb = jax.random.fold_in(key, 11)
    key_col = jax.random.fold_in(key, 12)
    key_own = jax.random.fold_in(key, 13)
    orb_scale = jnp.exp(jax.random.uniform(key_orb, (NORB, 1, 1, 1), jnp.float32, jnp.log(0.3), jnp.log(3.0)))
    col_scale = jnp.exp(jax.random.uniform(key_col, (1, NX, NY, 1), jnp.float32, jnp.log(0.5), jnp.log(5.0)))
    values = jax.random.truncated_normal(key_own, -4.0, 4.0, (NORB, NX, NY, NZ), jnp.float32)
    return (values * orb_scale * col_scale).astype(jnp.float32)


def set_ends(entries, rng, least, top_value):
    spot = [jax.random.randint(jax.random.fold_in(rng, axis), (), 0, length) for axis, length in enumerate(entries.shape)]
    longest = entries.shape.index(max(entries.shape))
    beside = spot[:longest] + [(spot[longest] + 1) % entries.shape[longest]] + spot[longest + 1:]
    return entries.at[tuple(spot)].set(least).at[tuple(beside)].set(top_value)


def level_of(own_key, extent, cuts, smallest, high):
    level = 1.0
    for dim, blocks in cuts:
        heights = jax.random.uniform(jax.random.fold_in(jax.random.fold_in(own_key, 6), dim), (blocks,), jnp.float32, smallest / len(cuts), high / len(cuts))
        level = level * jnp.repeat(jnp.exp(heights), extent[dim] // blocks).reshape((-1,) + (1,) * (len(extent) - 1 - dim))
    return level


def setup_inputs(seed: int = 0) -> dict:
    key_of = jax.random.split(jax.random.key(seed), 5)
    return {
        "orbitals": draw_orbitals(jax.random.fold_in(key_of[4], 71), 0),
        "potential": jnp.clip(jnp.exp(math.log(2.0) - 2.3025851 * jax.random.uniform(key_of[1], (NX, NY, NZ), jnp.float32) ** level_of(key_of[1], (NX, NY, NZ), ((0, 32), (1, 16)), -0.2, 0.2)), 0.2, 2.0),
        "sign_bits": set_ends(jax.random.randint(key_of[2], (NX, NY, NZ), 0, 2), jax.random.fold_in(key_of[2], 1), 0, 1).astype(jnp.int32),
        "sampled_rows": jax.vmap(lambda own: jax.random.permutation(own, CELLS_DEV))(jax.random.split(key_of[3], N_GX * N_GY)).reshape((N_GX, N_GY, CELLS_DEV)).astype(jnp.int32),
    }


HIGHEST = lax.Precision.HIGHEST
filter_center = 6.25
filter_half = 4.25

def hadamard_table(order):
    index = jnp.arange(order, dtype=jnp.int32)
    parity = jnp.zeros((order, order), jnp.int32)
    for bit in range(order.bit_length() - 1):
        weight = 2 ** bit
        parity = parity + index[:, None] // weight % 2 * (index[None, :] // weight % 2)
    return (1 - 2 * (parity % 2)).astype(jnp.float32)

def second_diff(padded, axis, count):
    parts = [lax.slice_in_dim(padded, k, k + count, axis=axis) for k in range(5)]
    return (16.0 * (parts[1] + parts[3]) - (parts[0] + parts[4]) - 30.0 * parts[2]) / 12.0

def apply_ham(field, potential):
    padded = jnp.pad(field, ((0, 0), (2, 2), (2, 2), (2, 2)))
    total = second_diff(padded[:, :, 2:-2, 2:-2], 1, field.shape[1])
    total = total + second_diff(padded[:, 2:-2, :, 2:-2], 2, field.shape[2])
    total = total + second_diff(padded[:, 2:-2, 2:-2, :], 3, field.shape[3])
    return -0.5 * total + potential[None] * field

def chebyshev(orbitals, potential):
    first = (apply_ham(orbitals, potential) - filter_center * orbitals) / filter_half
    second = 2.0 * (apply_ham(first, potential) - filter_center * first) / filter_half - orbitals
    return 2.0 * (apply_ham(second, potential) - filter_center * second) / filter_half - first

def transform_block(block, sign_block, rows, small, large):
    count = block.shape[0]
    flat = (block * sign_block[None]).reshape(count, -1, 128)
    mixed = jnp.einsum('nac,cd->nad', flat, small, precision=HIGHEST)
    mixed = jnp.einsum('ba,nac->nbc', large, mixed, precision=HIGHEST)
    mixed = mixed.reshape(count, -1)
    return jnp.take(mixed, rows, axis=1)

def reference(orbitals, potential, sign_bits, sampled_rows):
    filtered = chebyshev(orbitals, potential)
    applied = apply_ham(filtered, potential)
    stacked = jnp.concatenate([filtered, applied], axis=0)
    sign_field = (2 * sign_bits - 1).astype(jnp.float32)
    small = hadamard_table(128)
    large = hadamard_table(CELLS_DEV // 128)
    blocks = N_GX * N_GY

    def add_block(number, acc):
        number = jnp.asarray(number).astype(jnp.int32)
        row_x = (number // N_GY).astype(jnp.int32)
        row_y = (number % N_GY).astype(jnp.int32)
        zero = jnp.zeros((), jnp.int32)
        block = lax.dynamic_slice(stacked, (zero, row_x * CX, row_y * CY, zero), (2 * NORB, CX, CY, NZ))
        sign_block = lax.dynamic_slice(sign_field, (row_x * CX, row_y * CY, zero), (CX, CY, NZ))
        rows = lax.dynamic_slice(sampled_rows, (row_x, row_y, zero), (1, 1, M))[0, 0]
        return acc + transform_block(block, sign_block, rows, small, large)
    acc = lax.fori_loop(0, blocks, add_block, jnp.zeros((2 * NORB, M), jnp.float32))
    sketches = (acc / jnp.sqrt(jnp.float32(M * blocks))).reshape(2, NORB, M)
    gram = jnp.dot(sketches[0], sketches[0].T, precision=HIGHEST) / CELLS_DEV
    cross = jnp.dot(sketches[0], sketches[1].T, precision=HIGHEST) / CELLS_DEV
    lower = jnp.linalg.cholesky(gram)
    inverse = lax.linalg.triangular_solve(lower, jnp.eye(NORB, dtype=jnp.float32), left_side=True, lower=True)
    rotated = jnp.dot(inverse, filtered.reshape(NORB, -1), precision=HIGHEST).reshape(filtered.shape)
    inner = jnp.dot(jnp.dot(inverse, cross, precision=HIGHEST), inverse.T, precision=HIGHEST)
    projected = 0.5 * (inner + inner.T)
    return (rotated, sketches, projected)
```

```python
import jax
import jax.numpy as jnp
from jax import lax
from jax.sharding import PartitionSpec as P

M = 4096


HIGHEST = lax.Precision.HIGHEST
filter_center = 6.25
filter_half = 4.25


def halos(array, axis, dim, width):
    size, length = (lax.axis_size(axis), array.shape[dim])
    up = [(i, (i + 1) % size) for i in range(size - 1)]
    down = [(j, i) for i, j in up]
    last = lax.slice_in_dim(array, length - width, length, axis=dim)
    initial = lax.slice_in_dim(array, 0, width, axis=dim)
    before = lax.ppermute(last, axis, up)
    after = lax.ppermute(initial, axis, down)
    return before, after


STAGES = (("gx", 0), ("gx", 1), ("gy", 0), ("gy", 2), ("gx", 2), ("gy", 1), ("gy", 3), ("gx", 3), ("gx", 4))


def axis_bits(axis):
    return lax.axis_size(axis).bit_length() - 1


def butterfly_scatter(x):
    n, cols = x.shape
    nbx, nby = axis_bits("gx"), axis_bits("gy")
    rest = cols >> (nbx + nby)
    buf = x.reshape((n,) + (2,) * (nbx + nby) + (rest,))
    dims = {("gx", b): nbx - b for b in range(nbx)}
    dims.update({("gy", b): nbx + nby - b for b in range(nby)})
    live = list(range(buf.ndim))
    for axis, b in STAGES:
        d = live.index(dims[(axis, b)])
        mine = (lax.axis_index(axis) // (2**b)) % 2
        keep = lax.dynamic_index_in_dim(buf, mine, d, keepdims=False)
        send = lax.dynamic_index_in_dim(buf, 1 - mine, d, keepdims=False)
        pairs = [(k, k ^ (2**b)) for k in range(lax.axis_size(axis))]
        buf = keep + lax.ppermute(send, axis, pairs)
        live.pop(d)
    return buf.reshape(n, rest)


def butterfly_sum(x):
    for axis, b in STAGES:
        pairs = [(k, k ^ (2**b)) for k in range(lax.axis_size(axis))]
        x = x + lax.ppermute(x, axis, pairs)
    return x


def hadamard_table(order):
    index = jnp.arange(order, dtype=jnp.int32)
    parity = jnp.zeros((order, order), jnp.int32)
    for bit in range(order.bit_length() - 1):
        weight = 2**bit
        parity = parity + index[:, None] // weight % 2 * (index[None, :] // weight % 2)
    return (1 - 2 * (parity % 2)).astype(jnp.float32)


def second_diff(padded, axis, count):
    parts = [lax.slice_in_dim(padded, k, k + count, axis=axis) for k in range(5)]
    return (16.0 * (parts[1] + parts[3]) - (parts[0] + parts[4]) - 30.0 * parts[2]) / 12.0


def apply_ham(field, potential):
    x_before, x_after = halos(field, "gx", 1, 2)
    y_before, y_after = halos(field, "gy", 2, 2)
    x_padded = jnp.concatenate([x_before, field, x_after], axis=1)
    y_padded = jnp.concatenate([y_before, field, y_after], axis=2)
    z_padded = jnp.pad(field, ((0, 0), (0, 0), (0, 0), (2, 2)))
    total = second_diff(x_padded, 1, field.shape[1])
    total = total + second_diff(y_padded, 2, field.shape[2])
    total = total + second_diff(z_padded, 3, field.shape[3])
    return -0.5 * total + potential[None] * field


def shards(orbitals, potential, sign_bits, sampled_rows):
    first = (apply_ham(orbitals, potential) - filter_center * orbitals) / filter_half
    second = 2.0 * (apply_ham(first, potential) - filter_center * first) / filter_half - orbitals
    filtered = 2.0 * (apply_ham(second, potential) - filter_center * second) / filter_half - first
    applied = apply_ham(filtered, potential)
    count = orbitals.shape[0]
    cells = orbitals.shape[1] * orbitals.shape[2] * orbitals.shape[3]
    stacked = jnp.concatenate([filtered, applied], axis=0)
    sign_block = (2 * sign_bits - 1).astype(jnp.float32)
    flat = (stacked * sign_block[None]).reshape(2 * count, -1, 128)
    mixed = jnp.einsum("nac,cd->nad", flat, hadamard_table(128), precision=HIGHEST)
    mixed = jnp.einsum("ba,nac->nbc", hadamard_table(cells // 128), mixed, precision=HIGHEST)
    mixed = mixed.reshape(2 * count, cells)
    picked = jnp.take(mixed, sampled_rows[0, 0, :M], axis=1)
    devices = lax.axis_size("gx") * lax.axis_size("gy")
    term = (picked / jnp.sqrt(jnp.float32(M * devices))).reshape(2, count, M)
    assert len(STAGES) == axis_bits("gx") + axis_bits("gy")
    share = butterfly_scatter(term.reshape(2 * count, M)).reshape(2, count, -1)
    part_gram = jnp.dot(share[0], share[0].T, precision=HIGHEST)
    part_cross = jnp.dot(share[0], share[1].T, precision=HIGHEST)
    parts = butterfly_sum(jnp.stack([part_gram, part_cross])) / cells
    gram, cross = parts[0], parts[1]
    lower = jnp.linalg.cholesky(gram)
    inverse = lax.linalg.triangular_solve(
        lower, jnp.eye(count, dtype=jnp.float32), left_side=True, lower=True
    )
    rotated = jnp.dot(inverse, filtered.reshape(count, -1), precision=HIGHEST).reshape(
        filtered.shape
    )
    inner = jnp.dot(jnp.dot(inverse, cross, precision=HIGHEST), inverse.T, precision=HIGHEST)
    projected = 0.5 * (inner + inner.T)
    return (rotated, share, projected)


def solution(mesh):
    in_specs = (
        P(None, "gx", "gy", None),
        P("gx", "gy", None),
        P("gx", "gy", None),
        P("gx", "gy", None),
    )
    out_specs = (P(None, "gx", "gy", None), P(None, None, ("gx", "gy")), P())
    return jax.shard_map(shards, mesh=mesh, in_specs=in_specs, out_specs=out_specs, check_vma=False)
```

```python
import jax
import jax.numpy as jnp
from jax import lax
from jax.sharding import Mesh, PartitionSpec as P

M = 4096


HIGHEST = lax.Precision.HIGHEST
filter_center = 6.25
filter_half = 4.25


def halos(array, axis, dim, width):
    size, length = (lax.axis_size(axis), array.shape[dim])
    up = [(i, (i + 1) % size) for i in range(size - 1)]
    down = [(j, i) for i, j in up]
    last = lax.slice_in_dim(array, length - width, length, axis=dim)
    initial = lax.slice_in_dim(array, 0, width, axis=dim)
    before = lax.ppermute(last, axis, up)
    after = lax.ppermute(initial, axis, down)
    return before, after


STAGES = (("xl", 0), ("xl", 1), ("gy", 0), ("gy", 2), ("xl", 2), ("gy", 1), ("gy", 3), ("zh", 0), ("zh", 1))
BLOCK_AXES = ("zh", "xl", "gy")


def axis_bits(axis):
    return lax.axis_size(axis).bit_length() - 1


def butterfly_scatter(x):
    n, cols = x.shape
    bits = [axis_bits(axis) for axis in BLOCK_AXES]
    rest = cols >> sum(bits)
    buf = x.reshape((n,) + (2,) * sum(bits) + (rest,))
    dims, offset = {}, 1
    for axis, nb in zip(BLOCK_AXES, bits):
        dims.update({(axis, b): offset + nb - 1 - b for b in range(nb)})
        offset += nb
    live = list(range(buf.ndim))
    for axis, b in STAGES:
        d = live.index(dims[(axis, b)])
        mine = (lax.axis_index(axis) // (2**b)) % 2
        keep = lax.dynamic_index_in_dim(buf, mine, d, keepdims=False)
        send = lax.dynamic_index_in_dim(buf, 1 - mine, d, keepdims=False)
        pairs = [(k, k ^ (2**b)) for k in range(lax.axis_size(axis))]
        buf = keep + lax.ppermute(send, axis, pairs)
        live.pop(d)
    return buf.reshape(n, rest)


def butterfly_sum(x):
    for axis, b in STAGES:
        pairs = [(k, k ^ (2**b)) for k in range(lax.axis_size(axis))]
        x = x + lax.ppermute(x, axis, pairs)
    return x


def hadamard_table(order):
    index = jnp.arange(order, dtype=jnp.int32)
    parity = jnp.zeros((order, order), jnp.int32)
    for bit in range(order.bit_length() - 1):
        weight = 2**bit
        parity = parity + index[:, None] // weight % 2 * (index[None, :] // weight % 2)
    return (1 - 2 * (parity % 2)).astype(jnp.float32)


def second_diff(padded, axis, count):
    parts = [lax.slice_in_dim(padded, k, k + count, axis=axis) for k in range(5)]
    return (16.0 * (parts[1] + parts[3]) - (parts[0] + parts[4]) - 30.0 * parts[2]) / 12.0


def apply_ham(field, potential):
    x_before, x_after = halos(field, "zh", 1, 2)
    y_before, y_after = halos(field, "gy", 2, 2)
    x_padded = jnp.concatenate([x_before, field, x_after], axis=1)
    y_padded = jnp.concatenate([y_before, field, y_after], axis=2)
    z_padded = jnp.pad(field, ((0, 0), (0, 0), (0, 0), (2, 2)))
    total = second_diff(x_padded, 1, field.shape[1])
    total = total + second_diff(y_padded, 2, field.shape[2])
    total = total + second_diff(z_padded, 3, field.shape[3])
    return -0.5 * total + potential[None] * field


def shards(orbitals, potential, sign_bits, sampled_rows):
    group_potential = lax.all_gather(potential, "xl", axis=0, tiled=True)
    spread = lax.all_to_all(orbitals, "xl", 0, 1, tiled=True)
    first = (apply_ham(spread, group_potential) - filter_center * spread) / filter_half
    second = 2.0 * (apply_ham(first, group_potential) - filter_center * first) / filter_half - spread
    spread_filtered = (
        2.0 * (apply_ham(second, group_potential) - filter_center * second) / filter_half - first
    )
    spread_applied = apply_ham(spread_filtered, group_potential)
    filtered = lax.all_to_all(spread_filtered, "xl", 1, 0, tiled=True)
    applied = lax.all_to_all(spread_applied, "xl", 1, 0, tiled=True)
    count = orbitals.shape[0]
    cells = orbitals.shape[1] * orbitals.shape[2] * orbitals.shape[3]
    stacked = jnp.concatenate([filtered, applied], axis=0)
    sign_block = (2 * sign_bits - 1).astype(jnp.float32)
    flat = (stacked * sign_block[None]).reshape(2 * count, -1, 128)
    mixed = jnp.einsum("nac,cd->nad", flat, hadamard_table(128), precision=HIGHEST)
    mixed = jnp.einsum("ba,nac->nbc", hadamard_table(cells // 128), mixed, precision=HIGHEST)
    mixed = mixed.reshape(2 * count, cells)
    picked = jnp.take(mixed, sampled_rows[0, 0, :M], axis=1)
    devices = lax.axis_size("zh") * lax.axis_size("xl") * lax.axis_size("gy")
    term = (picked / jnp.sqrt(jnp.float32(M * devices))).reshape(2, count, M)
    assert len(STAGES) == sum(axis_bits(axis) for axis in BLOCK_AXES)
    share = butterfly_scatter(term.reshape(2 * count, M)).reshape(2, count, -1)
    part_gram = jnp.dot(share[0], share[0].T, precision=HIGHEST)
    part_cross = jnp.dot(share[0], share[1].T, precision=HIGHEST)
    parts = butterfly_sum(jnp.stack([part_gram, part_cross])) / cells
    gram, cross = parts[0], parts[1]
    lower = jnp.linalg.cholesky(gram)
    inverse = lax.linalg.triangular_solve(
        lower, jnp.eye(count, dtype=jnp.float32), left_side=True, lower=True
    )
    rotated = jnp.dot(inverse, filtered.reshape(count, -1), precision=HIGHEST).reshape(
        filtered.shape
    )
    inner = jnp.dot(jnp.dot(inverse, cross, precision=HIGHEST), inverse.T, precision=HIGHEST)
    projected = 0.5 * (inner + inner.T)
    return (rotated, share, projected)


def solution(mesh):
    groups = 4
    inner = Mesh(
        mesh.devices.reshape(groups, mesh.shape["gx"] // groups, mesh.shape["gy"]), ("zh", "xl", "gy")
    )
    gx = ("zh", "xl")
    in_specs = (
        P(None, gx, "gy", None),
        P(gx, "gy", None),
        P(gx, "gy", None),
        P(gx, "gy", None),
    )
    out_specs = (P(None, gx, "gy", None), P(None, None, gx + ("gy",)), P())
    return jax.shard_map(shards, mesh=inner, in_specs=in_specs, out_specs=out_specs, check_vma=False)
```

```python
import jax
import jax.numpy as jnp
from jax import lax
from jax.sharding import Mesh, PartitionSpec as P

M = 4096


HIGHEST = lax.Precision.HIGHEST
filter_center = 6.25
filter_half = 4.25


def halos(array, axis, dim, width):
    size, length = (lax.axis_size(axis), array.shape[dim])
    up = [(i, (i + 1) % size) for i in range(size - 1)]
    down = [(j, i) for i, j in up]
    last = lax.slice_in_dim(array, length - width, length, axis=dim)
    initial = lax.slice_in_dim(array, 0, width, axis=dim)
    before = lax.ppermute(last, axis, up)
    after = lax.ppermute(initial, axis, down)
    return before, after


BLOCK_AXES = ("zh", "xl", "gy")


def exchange_scatter(x):
    n = x.shape[0]
    zh, xl, gy = (lax.axis_size(axis) for axis in BLOCK_AXES)
    y = x.reshape(n, zh, xl, gy, -1).transpose(0, 2, 1, 3, 4)
    y = lax.all_to_all(y, "xl", 1, 1, tiled=True).sum(1)
    y = lax.all_to_all(y.transpose(0, 2, 1, 3), "gy", 1, 1, tiled=True).sum(1)
    return lax.all_to_all(y, "zh", 1, 1, tiled=True).sum(1)


def exchange_sum(x):
    for axis in ("xl", "gy", "zh"):
        size = lax.axis_size(axis)
        copies = jnp.broadcast_to(x[None], (size,) + x.shape)
        x = lax.all_to_all(copies, axis, 0, 0, tiled=True).sum(0)
    return x


def hadamard_table(order):
    index = jnp.arange(order, dtype=jnp.int32)
    parity = jnp.zeros((order, order), jnp.int32)
    for bit in range(order.bit_length() - 1):
        weight = 2**bit
        parity = parity + index[:, None] // weight % 2 * (index[None, :] // weight % 2)
    return (1 - 2 * (parity % 2)).astype(jnp.float32)


def second_diff(padded, axis, count):
    parts = [lax.slice_in_dim(padded, k, k + count, axis=axis) for k in range(5)]
    return (16.0 * (parts[1] + parts[3]) - (parts[0] + parts[4]) - 30.0 * parts[2]) / 12.0


def apply_ham(field, potential):
    x_before, x_after = halos(field, "zh", 1, 2)
    y_before, y_after = halos(field, "gy", 2, 2)
    x_padded = jnp.concatenate([x_before, field, x_after], axis=1)
    y_padded = jnp.concatenate([y_before, field, y_after], axis=2)
    z_padded = jnp.pad(field, ((0, 0), (0, 0), (0, 0), (2, 2)))
    total = second_diff(x_padded, 1, field.shape[1])
    total = total + second_diff(y_padded, 2, field.shape[2])
    total = total + second_diff(z_padded, 3, field.shape[3])
    return -0.5 * total + potential[None] * field


def shards(orbitals, potential, sign_bits, sampled_rows):
    chunks = lax.axis_size("xl")
    count = orbitals.shape[0]
    rows = orbitals.reshape((chunks, count // chunks) + orbitals.shape[1:])
    extra = jnp.broadcast_to(potential[None, None], (chunks, 1) + potential.shape)
    both = jnp.concatenate([rows, extra], axis=1).reshape((-1,) + orbitals.shape[1:])
    both = lax.all_to_all(both, "xl", 0, 1, tiled=True)
    spread, group_potential = both[: count // chunks], both[count // chunks]
    first = (apply_ham(spread, group_potential) - filter_center * spread) / filter_half
    second = 2.0 * (apply_ham(first, group_potential) - filter_center * first) / filter_half - spread
    spread_filtered = (
        2.0 * (apply_ham(second, group_potential) - filter_center * second) / filter_half - first
    )
    spread_applied = apply_ham(spread_filtered, group_potential)
    filtered = lax.all_to_all(spread_filtered, "xl", 1, 0, tiled=True)
    applied = lax.all_to_all(spread_applied, "xl", 1, 0, tiled=True)
    count = orbitals.shape[0]
    cells = orbitals.shape[1] * orbitals.shape[2] * orbitals.shape[3]
    stacked = jnp.concatenate([filtered, applied], axis=0)
    sign_block = (2 * sign_bits - 1).astype(jnp.float32)
    flat = (stacked * sign_block[None]).reshape(2 * count, -1, 128)
    mixed = jnp.einsum("nac,cd->nad", flat, hadamard_table(128), precision=HIGHEST)
    mixed = jnp.einsum("ba,nac->nbc", hadamard_table(cells // 128), mixed, precision=HIGHEST)
    mixed = mixed.reshape(2 * count, cells)
    picked = jnp.take(mixed, sampled_rows[0, 0, :M], axis=1)
    devices = lax.axis_size("zh") * lax.axis_size("xl") * lax.axis_size("gy")
    term = (picked / jnp.sqrt(jnp.float32(M * devices))).reshape(2, count, M)
    share = exchange_scatter(term.reshape(2 * count, M)).reshape(2, count, -1)
    part_gram = jnp.dot(share[0], share[0].T, precision=HIGHEST)
    part_cross = jnp.dot(share[0], share[1].T, precision=HIGHEST)
    parts = exchange_sum(jnp.stack([part_gram, part_cross])) / cells
    gram, cross = parts[0], parts[1]
    lower = jnp.linalg.cholesky(gram)
    inverse = lax.linalg.triangular_solve(
        lower, jnp.eye(count, dtype=jnp.float32), left_side=True, lower=True
    )
    rotated = jnp.dot(inverse, filtered.reshape(count, -1), precision=HIGHEST).reshape(
        filtered.shape
    )
    inner = jnp.dot(jnp.dot(inverse, cross, precision=HIGHEST), inverse.T, precision=HIGHEST)
    projected = 0.5 * (inner + inner.T)
    return (rotated, share, projected)


def solution(mesh):
    groups = 4
    inner = Mesh(
        mesh.devices.reshape(groups, mesh.shape["gx"] // groups, mesh.shape["gy"]), ("zh", "xl", "gy")
    )
    gx = ("zh", "xl")
    in_specs = (
        P(None, gx, "gy", None),
        P(gx, "gy", None),
        P(gx, "gy", None),
        P(gx, "gy", None),
    )
    out_specs = (P(None, gx, "gy", None), P(None, None, gx + ("gy",)), P())
    return jax.shard_map(shards, mesh=inner, in_specs=in_specs, out_specs=out_specs, check_vma=False)
```

```python
import jax
import jax.numpy as jnp
from jax import lax
from jax.sharding import Mesh, PartitionSpec as P

M = 4096


HIGHEST = lax.Precision.HIGHEST
filter_center = 6.25
filter_half = 4.25


def halos(array, axis, dim, width):
    size, length = (lax.axis_size(axis), array.shape[dim])
    up = [(i, (i + 1) % size) for i in range(size - 1)]
    down = [(j, i) for i, j in up]
    last = lax.slice_in_dim(array, length - width, length, axis=dim)
    initial = lax.slice_in_dim(array, 0, width, axis=dim)
    before = lax.ppermute(last, axis, up)
    after = lax.ppermute(initial, axis, down)
    return before, after


def corner(array, dx, dy, width):
    sx, sy = lax.axis_size("zh"), lax.axis_size("gy")
    xs = slice(array.shape[1] - width, None) if dx > 0 else slice(0, width)
    ys = slice(array.shape[2] - width, None) if dy > 0 else slice(0, width)
    pairs = [
        (k * sy + j, (k + dx) * sy + (j + dy))
        for k in range(sx)
        for j in range(sy)
        if 0 <= k + dx < sx and 0 <= j + dy < sy
    ]
    return lax.ppermute(array[:, xs, ys], ("zh", "gy"), pairs)


def exchange(field, width):
    x_before, x_after = halos(field, "zh", 1, width)
    y_before, y_after = halos(field, "gy", 2, width)
    top = [corner(field, 1, 1, width), x_before, corner(field, 1, -1, width)]
    bottom = [corner(field, -1, 1, width), x_after, corner(field, -1, -1, width)]
    rows = [
        jnp.concatenate(top, axis=2),
        jnp.concatenate([y_before, field, y_after], axis=2),
        jnp.concatenate(bottom, axis=2),
    ]
    return jnp.concatenate(rows, axis=1)


def on_grid(field, width):
    sx, sy = lax.axis_size("zh"), lax.axis_size("gy")
    inner_x, inner_y = field.shape[1] - 2 * width, field.shape[2] - 2 * width
    x = lax.axis_index("zh") * inner_x - width + lax.broadcasted_iota(jnp.int32, field.shape[1:3], 0)
    y = lax.axis_index("gy") * inner_y - width + lax.broadcasted_iota(jnp.int32, field.shape[1:3], 1)
    inside = (x >= 0) & (x < sx * inner_x) & (y >= 0) & (y < sy * inner_y)
    return jnp.where(inside[None, :, :, None], field, 0.0)


def ham_inside(padded, potential):
    core = padded[:, 2:-2, 2:-2]
    total = second_diff(padded[:, :, 2:-2], 1, core.shape[1])
    total = total + second_diff(padded[:, 2:-2, :], 2, core.shape[2])
    z_padded = jnp.pad(core, ((0, 0), (0, 0), (0, 0), (2, 2)))
    total = total + second_diff(z_padded, 3, core.shape[3])
    return -0.5 * total + potential[None] * core


BLOCK_AXES = ("zh", "xl", "gy")


def exchange_scatter(x):
    n = x.shape[0]
    zh, xl, gy = (lax.axis_size(axis) for axis in BLOCK_AXES)
    y = x.reshape(n, zh, xl, gy, -1).transpose(0, 2, 1, 3, 4)
    y = lax.all_to_all(y, "xl", 1, 1, tiled=True).sum(1)
    y = lax.all_to_all(y.transpose(0, 2, 1, 3), "gy", 1, 1, tiled=True).sum(1)
    return lax.all_to_all(y, "zh", 1, 1, tiled=True).sum(1)


def exchange_sum(x):
    for axis in ("xl", "gy", "zh"):
        size = lax.axis_size(axis)
        copies = jnp.broadcast_to(x[None], (size,) + x.shape)
        x = lax.all_to_all(copies, axis, 0, 0, tiled=True).sum(0)
    return x


def hadamard_table(order):
    index = jnp.arange(order, dtype=jnp.int32)
    parity = jnp.zeros((order, order), jnp.int32)
    for bit in range(order.bit_length() - 1):
        weight = 2**bit
        parity = parity + index[:, None] // weight % 2 * (index[None, :] // weight % 2)
    return (1 - 2 * (parity % 2)).astype(jnp.float32)


def second_diff(padded, axis, count):
    parts = [lax.slice_in_dim(padded, k, k + count, axis=axis) for k in range(5)]
    return (16.0 * (parts[1] + parts[3]) - (parts[0] + parts[4]) - 30.0 * parts[2]) / 12.0


def apply_ham(field, potential):
    x_before, x_after = halos(field, "zh", 1, 2)
    y_before, y_after = halos(field, "gy", 2, 2)
    x_padded = jnp.concatenate([x_before, field, x_after], axis=1)
    y_padded = jnp.concatenate([y_before, field, y_after], axis=2)
    z_padded = jnp.pad(field, ((0, 0), (0, 0), (0, 0), (2, 2)))
    total = second_diff(x_padded, 1, field.shape[1])
    total = total + second_diff(y_padded, 2, field.shape[2])
    total = total + second_diff(z_padded, 3, field.shape[3])
    return -0.5 * total + potential[None] * field


def shards(orbitals, potential, sign_bits, sampled_rows):
    chunks = lax.axis_size("xl")
    count = orbitals.shape[0]
    rows = orbitals.reshape((chunks, count // chunks) + orbitals.shape[1:])
    extra = jnp.broadcast_to(potential[None, None], (chunks, 1) + potential.shape)
    both = jnp.concatenate([rows, extra], axis=1).reshape((-1,) + orbitals.shape[1:])
    both = lax.all_to_all(both, "xl", 0, 1, tiled=True)
    spread, group_potential = both[: count // chunks], both[count // chunks]
    wide = exchange(jnp.concatenate([spread, group_potential[None]], axis=0), 4)
    rings, wide_potential = wide[: count // chunks], wide[count // chunks, 2:-2, 2:-2]
    inner_potential = group_potential
    near = rings[:, 2:-2, 2:-2]
    first = on_grid((ham_inside(rings, wide_potential) - filter_center * near) / filter_half, 2)
    inner_first = first[:, 2:-2, 2:-2]
    second = (
        2.0 * (ham_inside(first, inner_potential) - filter_center * inner_first) / filter_half - spread
    )
    wide = exchange(jnp.concatenate([second, inner_first], axis=0), 4)
    second_rings, first_rings = wide[: count // chunks], wide[count // chunks :]
    near = second_rings[:, 2:-2, 2:-2]
    spread_filtered = on_grid(
        2.0 * (ham_inside(second_rings, wide_potential) - filter_center * near) / filter_half
        - first_rings[:, 2:-2, 2:-2],
        2,
    )
    spread_applied = ham_inside(spread_filtered, inner_potential)
    spread_filtered = spread_filtered[:, 2:-2, 2:-2]
    filtered = lax.all_to_all(spread_filtered, "xl", 1, 0, tiled=True)
    applied = lax.all_to_all(spread_applied, "xl", 1, 0, tiled=True)
    count = orbitals.shape[0]
    cells = orbitals.shape[1] * orbitals.shape[2] * orbitals.shape[3]
    stacked = jnp.concatenate([filtered, applied], axis=0)
    sign_block = (2 * sign_bits - 1).astype(jnp.float32)
    flat = (stacked * sign_block[None]).reshape(2 * count, -1, 128)
    mixed = jnp.einsum("nac,cd->nad", flat, hadamard_table(128), precision=HIGHEST)
    mixed = jnp.einsum("ba,nac->nbc", hadamard_table(cells // 128), mixed, precision=HIGHEST)
    mixed = mixed.reshape(2 * count, cells)
    picked = jnp.take(mixed, sampled_rows[0, 0, :M], axis=1)
    devices = lax.axis_size("zh") * lax.axis_size("xl") * lax.axis_size("gy")
    term = (picked / jnp.sqrt(jnp.float32(M * devices))).reshape(2, count, M)
    share = exchange_scatter(term.reshape(2 * count, M)).reshape(2, count, -1)
    part_gram = jnp.dot(share[0], share[0].T, precision=HIGHEST)
    part_cross = jnp.dot(share[0], share[1].T, precision=HIGHEST)
    parts = exchange_sum(jnp.stack([part_gram, part_cross])) / cells
    gram, cross = parts[0], parts[1]
    lower = jnp.linalg.cholesky(gram)
    inverse = lax.linalg.triangular_solve(
        lower, jnp.eye(count, dtype=jnp.float32), left_side=True, lower=True
    )
    rotated = jnp.dot(inverse, filtered.reshape(count, -1), precision=HIGHEST).reshape(
        filtered.shape
    )
    inner = jnp.dot(jnp.dot(inverse, cross, precision=HIGHEST), inverse.T, precision=HIGHEST)
    projected = 0.5 * (inner + inner.T)
    return (rotated, share, projected)


def solution(mesh):
    groups = 4
    inner = Mesh(
        mesh.devices.reshape(groups, mesh.shape["gx"] // groups, mesh.shape["gy"]), ("zh", "xl", "gy")
    )
    gx = ("zh", "xl")
    in_specs = (
        P(None, gx, "gy", None),
        P(gx, "gy", None),
        P(gx, "gy", None),
        P(gx, "gy", None),
    )
    out_specs = (P(None, gx, "gy", None), P(None, None, gx + ("gy",)), P())
    return jax.shard_map(shards, mesh=inner, in_specs=in_specs, out_specs=out_specs, check_vma=False)
```

```python
import jax
import jax.numpy as jnp
from jax import lax
from jax.sharding import Mesh, PartitionSpec as P

M = 4096


HIGHEST = lax.Precision.HIGHEST
filter_center = 6.25
filter_half = 4.25


def halos(array, axis, dim, width):
    size, length = (lax.axis_size(axis), array.shape[dim])
    up = [(i, (i + 1) % size) for i in range(size - 1)]
    down = [(j, i) for i, j in up]
    last = lax.slice_in_dim(array, length - width, length, axis=dim)
    initial = lax.slice_in_dim(array, 0, width, axis=dim)
    before = lax.ppermute(last, axis, up)
    after = lax.ppermute(initial, axis, down)
    return before, after


BLOCK_AXES = ("zh", "xl", "gy")


def exchange_scatter(x):
    n = x.shape[0]
    zh, xl, gy = (lax.axis_size(axis) for axis in BLOCK_AXES)
    y = x.reshape(n, zh, xl, gy, -1).transpose(0, 2, 1, 3, 4)
    y = lax.all_to_all(y, "xl", 1, 1, tiled=True).sum(1)
    y = lax.all_to_all(y.transpose(0, 2, 1, 3), "gy", 1, 1, tiled=True).sum(1)
    return lax.all_to_all(y, "zh", 1, 1, tiled=True).sum(1)


def exchange_sum(x):
    for axis in ("xl", "gy", "zh"):
        size = lax.axis_size(axis)
        copies = jnp.broadcast_to(x[None], (size,) + x.shape)
        x = lax.all_to_all(copies, axis, 0, 0, tiled=True).sum(0)
    return x


def hadamard_table(order):
    index = jnp.arange(order, dtype=jnp.int32)
    parity = jnp.zeros((order, order), jnp.int32)
    for bit in range(order.bit_length() - 1):
        weight = 2**bit
        parity = parity + index[:, None] // weight % 2 * (index[None, :] // weight % 2)
    return (1 - 2 * (parity % 2)).astype(jnp.float32)


def second_diff(padded, axis, count):
    parts = [lax.slice_in_dim(padded, k, k + count, axis=axis) for k in range(5)]
    return (16.0 * (parts[1] + parts[3]) - (parts[0] + parts[4]) - 30.0 * parts[2]) / 12.0


def apply_ham(field, potential):
    x_before, x_after = halos(field, "zh", 1, 2)
    y_before, y_after = halos(field, "gy", 2, 2)
    x_padded = jnp.concatenate([x_before, field, x_after], axis=1)
    y_padded = jnp.concatenate([y_before, field, y_after], axis=2)
    z_padded = jnp.pad(field, ((0, 0), (0, 0), (0, 0), (2, 2)))
    total = second_diff(x_padded, 1, field.shape[1])
    total = total + second_diff(y_padded, 2, field.shape[2])
    total = total + second_diff(z_padded, 3, field.shape[3])
    return -0.5 * total + potential[None] * field


def shards(orbitals, potential, sign_bits, sampled_rows):
    chunks = lax.axis_size("xl")
    count = orbitals.shape[0]
    own = count // chunks
    cells = orbitals.shape[1] * orbitals.shape[2] * orbitals.shape[3]
    sign_block = (2 * sign_bits - 1).astype(jnp.float32)
    picks = sampled_rows.reshape(potential.shape).astype(jnp.float32)
    rows = orbitals.reshape((chunks, own) + orbitals.shape[1:])
    extra = jnp.broadcast_to(
        jnp.stack([potential, sign_block, picks])[None], (chunks, 3) + potential.shape
    )
    both = jnp.concatenate([rows, extra], axis=1).reshape((-1,) + orbitals.shape[1:])
    both = lax.all_to_all(both, "xl", 0, 1, tiled=True)
    spread, group_potential, group_sign = both[:own], both[own], both[own + 1]
    group_picks = both[own + 2].reshape(chunks, cells)[:, :M].astype(jnp.int32)
    first = (apply_ham(spread, group_potential) - filter_center * spread) / filter_half
    second = 2.0 * (apply_ham(first, group_potential) - filter_center * first) / filter_half - spread
    spread_filtered = (
        2.0 * (apply_ham(second, group_potential) - filter_center * second) / filter_half - first
    )
    spread_applied = apply_ham(spread_filtered, group_potential)
    filtered = lax.all_to_all(spread_filtered, "xl", 1, 0, tiled=True)

    fields = jnp.concatenate([spread_filtered, spread_applied], axis=0) * group_sign[None]
    flat = fields.reshape((2 * own, chunks, cells)).transpose(1, 0, 2).reshape(-1, cells // 128, 128)
    mixed = jnp.einsum("nac,cd->nad", flat, hadamard_table(128), precision=HIGHEST)
    mixed = jnp.einsum("ba,nac->nbc", hadamard_table(cells // 128), mixed, precision=HIGHEST)
    mixed = mixed.reshape(chunks, 2 * own, cells)
    index = jnp.broadcast_to(group_picks[:, None, :], (chunks, 2 * own, M))
    picked = jnp.take_along_axis(mixed, index, axis=2).sum(0)
    devices = lax.axis_size("zh") * chunks * lax.axis_size("gy")
    term = picked / jnp.sqrt(jnp.float32(M * devices))

    zh, gy = lax.axis_size("zh"), lax.axis_size("gy")
    term = term.reshape(2 * own, zh, chunks, gy, -1).transpose(2, 0, 1, 3, 4)
    term = lax.all_to_all(term, "xl", 0, 0, tiled=True)
    term = term.reshape((chunks, 2, own) + term.shape[2:]).transpose(1, 0, 2, 3, 4, 5)
    term = term.reshape(2 * count, zh, gy, -1).transpose(0, 2, 1, 3)
    term = lax.all_to_all(term, "gy", 1, 1, tiled=True).sum(1)
    term = lax.all_to_all(term, "zh", 1, 1, tiled=True).sum(1)
    share = term.reshape(2, count, -1)
    part_gram = jnp.dot(share[0], share[0].T, precision=HIGHEST)
    part_cross = jnp.dot(share[0], share[1].T, precision=HIGHEST)
    parts = exchange_sum(jnp.stack([part_gram, part_cross])) / cells
    gram, cross = parts[0], parts[1]
    lower = jnp.linalg.cholesky(gram)
    inverse = lax.linalg.triangular_solve(
        lower, jnp.eye(count, dtype=jnp.float32), left_side=True, lower=True
    )
    rotated = jnp.dot(inverse, filtered.reshape(count, -1), precision=HIGHEST).reshape(
        filtered.shape
    )
    inner = jnp.dot(jnp.dot(inverse, cross, precision=HIGHEST), inverse.T, precision=HIGHEST)
    projected = 0.5 * (inner + inner.T)
    return (rotated, share, projected)


def solution(mesh):
    groups = 4
    inner = Mesh(
        mesh.devices.reshape(groups, mesh.shape["gx"] // groups, mesh.shape["gy"]), ("zh", "xl", "gy")
    )
    gx = ("zh", "xl")
    in_specs = (
        P(None, gx, "gy", None),
        P(gx, "gy", None),
        P(gx, "gy", None),
        P(gx, "gy", None),
    )
    out_specs = (P(None, gx, "gy", None), P(None, None, gx + ("gy",)), P())
    return jax.shard_map(shards, mesh=inner, in_specs=in_specs, out_specs=out_specs, check_vma=False)
```

```python
import jax
import jax.numpy as jnp
from jax import lax
from jax.sharding import Mesh, PartitionSpec as P

M = 4096


HIGHEST = lax.Precision.HIGHEST
filter_center = 6.25
filter_half = 4.25


def halos(array, axis, dim, width):
    size, length = (lax.axis_size(axis), array.shape[dim])
    up = [(i, (i + 1) % size) for i in range(size - 1)]
    down = [(j, i) for i, j in up]
    last = lax.slice_in_dim(array, length - width, length, axis=dim)
    initial = lax.slice_in_dim(array, 0, width, axis=dim)
    before = lax.ppermute(last, axis, up)
    after = lax.ppermute(initial, axis, down)
    return before, after


BLOCK_AXES = ("zh", "xl", "gy")


def exchange_scatter(x):
    n = x.shape[0]
    zh, xl, gy = (lax.axis_size(axis) for axis in BLOCK_AXES)
    y = x.reshape(n, zh, xl, gy, -1).transpose(0, 2, 1, 3, 4)
    y = lax.all_to_all(y, "xl", 1, 1, tiled=True).sum(1)
    y = lax.all_to_all(y.transpose(0, 2, 1, 3), "gy", 1, 1, tiled=True).sum(1)
    return exchange_sum(y, ("zh",))


def exchange_sum(x, axes):
    for axis in axes:
        size = lax.axis_size(axis)
        copies = jnp.broadcast_to(x[None], (size,) + x.shape)
        x = lax.all_to_all(copies, axis, 0, 0, tiled=True).sum(0)
    return x


def hadamard_table(order):
    index = jnp.arange(order, dtype=jnp.int32)
    parity = jnp.zeros((order, order), jnp.int32)
    for bit in range(order.bit_length() - 1):
        weight = 2**bit
        parity = parity + index[:, None] // weight % 2 * (index[None, :] // weight % 2)
    return (1 - 2 * (parity % 2)).astype(jnp.float32)


def second_diff(padded, axis, count):
    parts = [lax.slice_in_dim(padded, k, k + count, axis=axis) for k in range(5)]
    return (16.0 * (parts[1] + parts[3]) - (parts[0] + parts[4]) - 30.0 * parts[2]) / 12.0


def apply_ham(field, potential):
    x_before, x_after = halos(field, "zh", 1, 2)
    y_before, y_after = halos(field, "gy", 2, 2)
    x_padded = jnp.concatenate([x_before, field, x_after], axis=1)
    y_padded = jnp.concatenate([y_before, field, y_after], axis=2)
    z_padded = jnp.pad(field, ((0, 0), (0, 0), (0, 0), (2, 2)))
    total = second_diff(x_padded, 1, field.shape[1])
    total = total + second_diff(y_padded, 2, field.shape[2])
    total = total + second_diff(z_padded, 3, field.shape[3])
    return -0.5 * total + potential[None] * field


def shards(orbitals, potential, sign_bits, sampled_rows):
    chunks = lax.axis_size("xl")
    count = orbitals.shape[0]
    rows = orbitals.reshape((chunks, count // chunks) + orbitals.shape[1:])
    extra = jnp.broadcast_to(potential[None, None], (chunks, 1) + potential.shape)
    both = jnp.concatenate([rows, extra], axis=1).reshape((-1,) + orbitals.shape[1:])
    both = lax.all_to_all(both, "xl", 0, 1, tiled=True)
    spread, group_potential = both[: count // chunks], both[count // chunks]
    first = (apply_ham(spread, group_potential) - filter_center * spread) / filter_half
    second = 2.0 * (apply_ham(first, group_potential) - filter_center * first) / filter_half - spread
    spread_filtered = (
        2.0 * (apply_ham(second, group_potential) - filter_center * second) / filter_half - first
    )
    spread_applied = apply_ham(spread_filtered, group_potential)
    filtered = lax.all_to_all(spread_filtered, "xl", 1, 0, tiled=True)
    applied = lax.all_to_all(spread_applied, "xl", 1, 0, tiled=True)
    count = orbitals.shape[0]
    cells = orbitals.shape[1] * orbitals.shape[2] * orbitals.shape[3]
    stacked = jnp.concatenate([filtered, applied], axis=0)
    sign_block = (2 * sign_bits - 1).astype(jnp.float32)
    flat = (stacked * sign_block[None]).reshape(2 * count, -1, 128)
    mixed = jnp.einsum("nac,cd->nad", flat, hadamard_table(128), precision=HIGHEST)
    mixed = jnp.einsum("ba,nac->nbc", hadamard_table(cells // 128), mixed, precision=HIGHEST)
    mixed = mixed.reshape(2 * count, cells)
    picked = jnp.take(mixed, sampled_rows[0, 0, :M], axis=1)
    devices = lax.axis_size("zh") * lax.axis_size("xl") * lax.axis_size("gy")
    term = (picked / jnp.sqrt(jnp.float32(M * devices))).reshape(2, count, M)
    summed = exchange_scatter(term.reshape(2 * count, M))
    share = lax.dynamic_index_in_dim(summed, lax.axis_index("zh"), 1, keepdims=False)
    share = share.reshape(2, count, -1)
    both = summed.reshape(2, count, -1)
    part_gram = jnp.dot(both[0], both[0].T, precision=HIGHEST)
    part_cross = jnp.dot(both[0], both[1].T, precision=HIGHEST)
    parts = exchange_sum(jnp.stack([part_gram, part_cross]), ("xl", "gy")) / cells
    gram, cross = parts[0], parts[1]
    lower = jnp.linalg.cholesky(gram)
    inverse = lax.linalg.triangular_solve(
        lower, jnp.eye(count, dtype=jnp.float32), left_side=True, lower=True
    )
    rotated = jnp.dot(inverse, filtered.reshape(count, -1), precision=HIGHEST).reshape(
        filtered.shape
    )
    inner = jnp.dot(jnp.dot(inverse, cross, precision=HIGHEST), inverse.T, precision=HIGHEST)
    projected = 0.5 * (inner + inner.T)
    return (rotated, share, projected)


def solution(mesh):
    groups = 4
    inner = Mesh(
        mesh.devices.reshape(groups, mesh.shape["gx"] // groups, mesh.shape["gy"]), ("zh", "xl", "gy")
    )
    gx = ("zh", "xl")
    in_specs = (
        P(None, gx, "gy", None),
        P(gx, "gy", None),
        P(gx, "gy", None),
        P(gx, "gy", None),
    )
    out_specs = (P(None, gx, "gy", None), P(None, None, gx + ("gy",)), P())
    return jax.shard_map(shards, mesh=inner, in_specs=in_specs, out_specs=out_specs, check_vma=False)
```

```python
import jax
import jax.numpy as jnp
from jax import lax
from jax.sharding import Mesh, PartitionSpec as P

M = 4096


HIGHEST = lax.Precision.HIGHEST
filter_center = 6.25
filter_half = 4.25


def halos(array, axis, dim, width):
    size, length = (lax.axis_size(axis), array.shape[dim])
    up = [(i, (i + 1) % size) for i in range(size - 1)]
    down = [(j, i) for i, j in up]
    last = lax.slice_in_dim(array, length - width, length, axis=dim)
    initial = lax.slice_in_dim(array, 0, width, axis=dim)
    before = lax.ppermute(last, axis, up)
    after = lax.ppermute(initial, axis, down)
    return before, after


BLOCK_AXES = ("zh", "xl", "gy")


def exchange_scatter(x):
    n = x.shape[0]
    zh, xl, gy = (lax.axis_size(axis) for axis in BLOCK_AXES)
    y = x.reshape(n, zh, xl * gy, -1).transpose(0, 2, 1, 3)
    y = lax.all_to_all(y, ("xl", "gy"), 1, 1, tiled=True).sum(1)
    return exchange_sum(y, ("zh",))


def exchange_sum(x, axes):
    for axis in axes:
        size = lax.axis_size(axis)
        copies = jnp.broadcast_to(x[None], (size,) + x.shape)
        x = lax.all_to_all(copies, axis, 0, 0, tiled=True).sum(0)
    return x


def hadamard_table(order):
    index = jnp.arange(order, dtype=jnp.int32)
    parity = jnp.zeros((order, order), jnp.int32)
    for bit in range(order.bit_length() - 1):
        weight = 2**bit
        parity = parity + index[:, None] // weight % 2 * (index[None, :] // weight % 2)
    return (1 - 2 * (parity % 2)).astype(jnp.float32)


def second_diff(padded, axis, count):
    parts = [lax.slice_in_dim(padded, k, k + count, axis=axis) for k in range(5)]
    return (16.0 * (parts[1] + parts[3]) - (parts[0] + parts[4]) - 30.0 * parts[2]) / 12.0


def apply_ham(field, potential):
    x_before, x_after = halos(field, "zh", 1, 2)
    y_before, y_after = halos(field, "gy", 2, 2)
    x_padded = jnp.concatenate([x_before, field, x_after], axis=1)
    y_padded = jnp.concatenate([y_before, field, y_after], axis=2)
    z_padded = jnp.pad(field, ((0, 0), (0, 0), (0, 0), (2, 2)))
    total = second_diff(x_padded, 1, field.shape[1])
    total = total + second_diff(y_padded, 2, field.shape[2])
    total = total + second_diff(z_padded, 3, field.shape[3])
    return -0.5 * total + potential[None] * field


def shards(orbitals, potential, sign_bits, sampled_rows):
    chunks = lax.axis_size("xl")
    count = orbitals.shape[0]
    rows = orbitals.reshape((chunks, count // chunks) + orbitals.shape[1:])
    extra = jnp.broadcast_to(potential[None, None], (chunks, 1) + potential.shape)
    both = jnp.concatenate([rows, extra], axis=1).reshape((-1,) + orbitals.shape[1:])
    both = lax.all_to_all(both, "xl", 0, 1, tiled=True)
    spread, group_potential = both[: count // chunks], both[count // chunks]
    first = (apply_ham(spread, group_potential) - filter_center * spread) / filter_half
    second = 2.0 * (apply_ham(first, group_potential) - filter_center * first) / filter_half - spread
    spread_filtered = (
        2.0 * (apply_ham(second, group_potential) - filter_center * second) / filter_half - first
    )
    spread_applied = apply_ham(spread_filtered, group_potential)
    filtered = lax.all_to_all(spread_filtered, "xl", 1, 0, tiled=True)
    applied = lax.all_to_all(spread_applied, "xl", 1, 0, tiled=True)
    count = orbitals.shape[0]
    cells = orbitals.shape[1] * orbitals.shape[2] * orbitals.shape[3]
    stacked = jnp.concatenate([filtered, applied], axis=0)
    sign_block = (2 * sign_bits - 1).astype(jnp.float32)
    flat = (stacked * sign_block[None]).reshape(2 * count, -1, 128)
    mixed = jnp.einsum("nac,cd->nad", flat, hadamard_table(128), precision=HIGHEST)
    mixed = jnp.einsum("ba,nac->nbc", hadamard_table(cells // 128), mixed, precision=HIGHEST)
    mixed = mixed.reshape(2 * count, cells)
    picked = jnp.take(mixed, sampled_rows[0, 0, :M], axis=1)
    devices = lax.axis_size("zh") * lax.axis_size("xl") * lax.axis_size("gy")
    term = (picked / jnp.sqrt(jnp.float32(M * devices))).reshape(2, count, M)
    summed = exchange_scatter(term.reshape(2 * count, M))
    share = lax.dynamic_index_in_dim(summed, lax.axis_index("zh"), 1, keepdims=False)
    share = share.reshape(2, count, -1)
    both = summed.reshape(2, count, -1)
    part_gram = jnp.dot(both[0], both[0].T, precision=HIGHEST)
    part_cross = jnp.dot(both[0], both[1].T, precision=HIGHEST)
    parts = exchange_sum(jnp.stack([part_gram, part_cross]), ("xl", "gy")) / cells
    gram, cross = parts[0], parts[1]
    lower = jnp.linalg.cholesky(gram)
    inverse = lax.linalg.triangular_solve(
        lower, jnp.eye(count, dtype=jnp.float32), left_side=True, lower=True
    )
    rotated = jnp.dot(inverse, filtered.reshape(count, -1), precision=HIGHEST).reshape(
        filtered.shape
    )
    inner = jnp.dot(jnp.dot(inverse, cross, precision=HIGHEST), inverse.T, precision=HIGHEST)
    projected = 0.5 * (inner + inner.T)
    return (rotated, share, projected)


def solution(mesh):
    groups = 4
    inner = Mesh(
        mesh.devices.reshape(groups, mesh.shape["gx"] // groups, mesh.shape["gy"]), ("zh", "xl", "gy")
    )
    gx = ("zh", "xl")
    in_specs = (
        P(None, gx, "gy", None),
        P(gx, "gy", None),
        P(gx, "gy", None),
        P(gx, "gy", None),
    )
    out_specs = (P(None, gx, "gy", None), P(None, None, gx + ("gy",)), P())
    return jax.shard_map(shards, mesh=inner, in_specs=in_specs, out_specs=out_specs, check_vma=False)
```

```python
import jax
import jax.numpy as jnp
from jax import lax
from jax.sharding import Mesh, PartitionSpec as P

M = 4096


HIGHEST = lax.Precision.HIGHEST
filter_center = 6.25
filter_half = 4.25


def halos(array, axis, dim, width):
    size, length = (lax.axis_size(axis), array.shape[dim])
    up = [(i, (i + 1) % size) for i in range(size - 1)]
    down = [(j, i) for i, j in up]
    last = lax.slice_in_dim(array, length - width, length, axis=dim)
    initial = lax.slice_in_dim(array, 0, width, axis=dim)
    before = lax.ppermute(last, axis, up)
    after = lax.ppermute(initial, axis, down)
    return before, after


BLOCK_AXES = ("zh", "xl", "gy")


def exchange_scatter(x):
    n = x.shape[0]
    zh, xl, gy = (lax.axis_size(axis) for axis in BLOCK_AXES)
    y = x.reshape(n, zh, xl, gy, -1).transpose(0, 2, 1, 3, 4)
    y = lax.all_to_all(y, "xl", 1, 1, tiled=True).sum(1)
    y = lax.all_to_all(y.transpose(0, 2, 1, 3), "gy", 1, 1, tiled=True).sum(1)
    return exchange_sum(y, ("zh",))


def exchange_sum(x, axes):
    for axis in axes:
        size = lax.axis_size(axis)
        copies = jnp.broadcast_to(x[None], (size,) + x.shape)
        x = lax.all_to_all(copies, axis, 0, 0, tiled=True).sum(0)
    return x


def hadamard_table(order):
    index = jnp.arange(order, dtype=jnp.int32)
    parity = jnp.zeros((order, order), jnp.int32)
    for bit in range(order.bit_length() - 1):
        weight = 2**bit
        parity = parity + index[:, None] // weight % 2 * (index[None, :] // weight % 2)
    return (1 - 2 * (parity % 2)).astype(jnp.float32)


def second_diff(padded, axis, count):
    parts = [lax.slice_in_dim(padded, k, k + count, axis=axis) for k in range(5)]
    return (16.0 * (parts[1] + parts[3]) - (parts[0] + parts[4]) - 30.0 * parts[2]) / 12.0


def apply_ham(field, potential):
    x_before, x_after = halos(field, "zh", 1, 2)
    y_before, y_after = halos(field, "gy", 2, 2)
    x_padded = jnp.concatenate([x_before, field, x_after], axis=1)
    y_padded = jnp.concatenate([y_before, field, y_after], axis=2)
    z_padded = jnp.pad(field, ((0, 0), (0, 0), (0, 0), (2, 2)))
    total = second_diff(x_padded, 1, field.shape[1])
    total = total + second_diff(y_padded, 2, field.shape[2])
    total = total + second_diff(z_padded, 3, field.shape[3])
    return -0.5 * total + potential[None] * field


def shards(orbitals, potential, sign_bits, sampled_rows):
    chunks = lax.axis_size("xl")
    count = orbitals.shape[0]
    rows = orbitals.reshape((chunks, count // chunks) + orbitals.shape[1:])
    extra = jnp.broadcast_to(potential[None, None], (chunks, 1) + potential.shape)
    both = jnp.concatenate([rows, extra], axis=1).reshape((-1,) + orbitals.shape[1:])
    both = lax.all_to_all(both, "xl", 0, 1, tiled=True)
    spread, group_potential = both[: count // chunks], both[count // chunks]
    first = (apply_ham(spread, group_potential) - filter_center * spread) / filter_half
    second = 2.0 * (apply_ham(first, group_potential) - filter_center * first) / filter_half - spread
    spread_filtered = (
        2.0 * (apply_ham(second, group_potential) - filter_center * second) / filter_half - first
    )
    spread_applied = apply_ham(spread_filtered, group_potential)
    filtered = lax.all_to_all(spread_filtered, "xl", 1, 0, tiled=True)
    applied = lax.all_to_all(spread_applied, "xl", 1, 0, tiled=True)
    count = orbitals.shape[0]
    cells = orbitals.shape[1] * orbitals.shape[2] * orbitals.shape[3]
    stacked = jnp.concatenate([filtered, applied], axis=0)
    sign_block = (2 * sign_bits - 1).astype(jnp.float32)
    flat = (stacked * sign_block[None]).reshape(2 * count, -1, 128)
    mixed = jnp.einsum("nac,cd->nad", flat, hadamard_table(128), precision=HIGHEST)
    mixed = jnp.einsum("ba,nac->bcn", hadamard_table(cells // 128), mixed, precision=HIGHEST)
    mixed = mixed.reshape(cells, 2 * count)
    picked = jnp.take(mixed, sampled_rows[0, 0, :M], axis=0).T
    devices = lax.axis_size("zh") * lax.axis_size("xl") * lax.axis_size("gy")
    term = (picked / jnp.sqrt(jnp.float32(M * devices))).reshape(2, count, M)
    summed = exchange_scatter(term.reshape(2 * count, M))
    share = lax.dynamic_index_in_dim(summed, lax.axis_index("zh"), 1, keepdims=False)
    share = share.reshape(2, count, -1)
    both = summed.reshape(2, count, -1)
    part_gram = jnp.dot(both[0], both[0].T, precision=HIGHEST)
    part_cross = jnp.dot(both[0], both[1].T, precision=HIGHEST)
    parts = exchange_sum(jnp.stack([part_gram, part_cross]), ("xl", "gy")) / cells
    gram, cross = parts[0], parts[1]
    lower = jnp.linalg.cholesky(gram)
    inverse = lax.linalg.triangular_solve(
        lower, jnp.eye(count, dtype=jnp.float32), left_side=True, lower=True
    )
    rotated = jnp.dot(inverse, filtered.reshape(count, -1), precision=HIGHEST).reshape(
        filtered.shape
    )
    inner = jnp.dot(jnp.dot(inverse, cross, precision=HIGHEST), inverse.T, precision=HIGHEST)
    projected = 0.5 * (inner + inner.T)
    return (rotated, share, projected)


def solution(mesh):
    groups = 4
    inner = Mesh(
        mesh.devices.reshape(groups, mesh.shape["gx"] // groups, mesh.shape["gy"]), ("zh", "xl", "gy")
    )
    gx = ("zh", "xl")
    in_specs = (
        P(None, gx, "gy", None),
        P(gx, "gy", None),
        P(gx, "gy", None),
        P(gx, "gy", None),
    )
    out_specs = (P(None, gx, "gy", None), P(None, None, gx + ("gy",)), P())
    return jax.shard_map(shards, mesh=inner, in_specs=in_specs, out_specs=out_specs, check_vma=False)
```

```python
import jax
import jax.numpy as jnp
from jax import lax
from jax.sharding import Mesh, PartitionSpec as P

M = 4096


HIGHEST = lax.Precision.HIGHEST
filter_center = 6.25
filter_half = 4.25


def halos(array, axis, dim, width):
    size, length = (lax.axis_size(axis), array.shape[dim])
    up = [(i, (i + 1) % size) for i in range(size - 1)]
    down = [(j, i) for i, j in up]
    last = lax.slice_in_dim(array, length - width, length, axis=dim)
    initial = lax.slice_in_dim(array, 0, width, axis=dim)
    before = lax.ppermute(last, axis, up)
    after = lax.ppermute(initial, axis, down)
    return before, after


BLOCK_AXES = ("zh", "xl", "gy")


def exchange_scatter(x):
    n = x.shape[0]
    zh, xl, gy = (lax.axis_size(axis) for axis in BLOCK_AXES)
    y = x.reshape(n, zh, xl, gy, -1).transpose(0, 2, 1, 3, 4)
    y = lax.all_to_all(y, "xl", 1, 1, tiled=True).sum(1)
    y = lax.all_to_all(y.transpose(0, 2, 1, 3), "gy", 1, 1, tiled=True).sum(1)
    return exchange_sum(y, ("zh",))


def exchange_sum(x, axes):
    for axis in axes:
        size = lax.axis_size(axis)
        copies = jnp.broadcast_to(x[None], (size,) + x.shape)
        x = lax.all_to_all(copies, axis, 0, 0, tiled=True).sum(0)
    return x


def hadamard_table(order):
    index = jnp.arange(order, dtype=jnp.int32)
    parity = jnp.zeros((order, order), jnp.int32)
    for bit in range(order.bit_length() - 1):
        weight = 2**bit
        parity = parity + index[:, None] // weight % 2 * (index[None, :] // weight % 2)
    return (1 - 2 * (parity % 2)).astype(jnp.float32)


def second_diff(padded, axis, count):
    parts = [lax.slice_in_dim(padded, k, k + count, axis=axis) for k in range(5)]
    return (16.0 * (parts[1] + parts[3]) - (parts[0] + parts[4]) - 30.0 * parts[2]) / 12.0


def apply_ham(field, potential):
    x_before, x_after = halos(field, "zh", 1, 2)
    y_before, y_after = halos(field, "gy", 2, 2)
    x_padded = jnp.concatenate([x_before, field, x_after], axis=1)
    y_padded = jnp.concatenate([y_before, field, y_after], axis=2)
    z_padded = jnp.pad(field, ((0, 0), (0, 0), (0, 0), (2, 2)))
    total = second_diff(x_padded, 1, field.shape[1])
    total = total + second_diff(y_padded, 2, field.shape[2])
    total = total + second_diff(z_padded, 3, field.shape[3])
    return -0.5 * total + potential[None] * field


def shards(orbitals, potential, sign_bits, sampled_rows):
    chunks = lax.axis_size("xl")
    count = orbitals.shape[0]
    rows = orbitals.reshape((chunks, count // chunks) + orbitals.shape[1:])
    extra = jnp.broadcast_to(potential[None, None], (chunks, 1) + potential.shape)
    both = jnp.concatenate([rows, extra], axis=1).reshape((-1,) + orbitals.shape[1:])
    both = lax.all_to_all(both, "xl", 0, 1, tiled=True)
    spread, group_potential = both[: count // chunks], both[count // chunks]
    first = (apply_ham(spread, group_potential) - filter_center * spread) / filter_half
    second = 2.0 * (apply_ham(first, group_potential) - filter_center * first) / filter_half - spread
    spread_filtered = (
        2.0 * (apply_ham(second, group_potential) - filter_center * second) / filter_half - first
    )
    spread_applied = apply_ham(spread_filtered, group_potential)
    filtered = lax.all_to_all(spread_filtered, "xl", 1, 0, tiled=True)
    applied = lax.all_to_all(spread_applied, "xl", 1, 0, tiled=True)
    count = orbitals.shape[0]
    cells = orbitals.shape[1] * orbitals.shape[2] * orbitals.shape[3]
    stacked = jnp.concatenate([filtered, applied], axis=0)
    sign_block = (2 * sign_bits - 1).astype(jnp.float32)
    flat = (stacked * sign_block[None]).reshape(2 * count, -1, 128)
    mixed = jnp.einsum("nac,cd->adn", flat, hadamard_table(128), precision=HIGHEST)
    mixed = jnp.einsum("ba,adn->bdn", hadamard_table(cells // 128), mixed, precision=HIGHEST)
    mixed = mixed.reshape(cells, 2 * count)
    picked = jnp.take(mixed, sampled_rows[0, 0, :M], axis=0).T
    devices = lax.axis_size("zh") * lax.axis_size("xl") * lax.axis_size("gy")
    term = (picked / jnp.sqrt(jnp.float32(M * devices))).reshape(2, count, M)
    summed = exchange_scatter(term.reshape(2 * count, M))
    share = lax.dynamic_index_in_dim(summed, lax.axis_index("zh"), 1, keepdims=False)
    share = share.reshape(2, count, -1)
    both = summed.reshape(2, count, -1)
    part_gram = jnp.dot(both[0], both[0].T, precision=HIGHEST)
    part_cross = jnp.dot(both[0], both[1].T, precision=HIGHEST)
    parts = exchange_sum(jnp.stack([part_gram, part_cross]), ("xl", "gy")) / cells
    gram, cross = parts[0], parts[1]
    lower = jnp.linalg.cholesky(gram)
    inverse = lax.linalg.triangular_solve(
        lower, jnp.eye(count, dtype=jnp.float32), left_side=True, lower=True
    )
    rotated = jnp.dot(inverse, filtered.reshape(count, -1), precision=HIGHEST).reshape(
        filtered.shape
    )
    inner = jnp.dot(jnp.dot(inverse, cross, precision=HIGHEST), inverse.T, precision=HIGHEST)
    projected = 0.5 * (inner + inner.T)
    return (rotated, share, projected)


def solution(mesh):
    groups = 4
    inner = Mesh(
        mesh.devices.reshape(groups, mesh.shape["gx"] // groups, mesh.shape["gy"]), ("zh", "xl", "gy")
    )
    gx = ("zh", "xl")
    in_specs = (
        P(None, gx, "gy", None),
        P(gx, "gy", None),
        P(gx, "gy", None),
        P(gx, "gy", None),
    )
    out_specs = (P(None, gx, "gy", None), P(None, None, gx + ("gy",)), P())
    return jax.shard_map(shards, mesh=inner, in_specs=in_specs, out_specs=out_specs, check_vma=False)
```

```python
import jax
import jax.numpy as jnp
from jax import lax
from jax.sharding import Mesh, PartitionSpec as P

M = 4096


HIGHEST = lax.Precision.HIGHEST
filter_center = 6.25
filter_half = 4.25


def halos(array, axis, dim, width):
    size, length = (lax.axis_size(axis), array.shape[dim])
    up = [(i, (i + 1) % size) for i in range(size - 1)]
    down = [(j, i) for i, j in up]
    last = lax.slice_in_dim(array, length - width, length, axis=dim)
    initial = lax.slice_in_dim(array, 0, width, axis=dim)
    before = lax.ppermute(last, axis, up)
    after = lax.ppermute(initial, axis, down)
    return before, after


BLOCK_AXES = ("zh", "xl", "gy")


def exchange_sum(x, axes):
    for axis in axes:
        size = lax.axis_size(axis)
        copies = jnp.broadcast_to(x[None], (size,) + x.shape)
        x = lax.all_to_all(copies, axis, 0, 0, tiled=True).sum(0)
    return x


def hadamard_table(order):
    index = jnp.arange(order, dtype=jnp.int32)
    parity = jnp.zeros((order, order), jnp.int32)
    for bit in range(order.bit_length() - 1):
        weight = 2**bit
        parity = parity + index[:, None] // weight % 2 * (index[None, :] // weight % 2)
    return (1 - 2 * (parity % 2)).astype(jnp.float32)


def second_diff(padded, axis, count):
    parts = [lax.slice_in_dim(padded, k, k + count, axis=axis) for k in range(5)]
    return (16.0 * (parts[1] + parts[3]) - (parts[0] + parts[4]) - 30.0 * parts[2]) / 12.0


def apply_ham(field, potential):
    x_before, x_after = halos(field, "zh", 1, 2)
    y_before, y_after = halos(field, "gy", 2, 2)
    x_padded = jnp.concatenate([x_before, field, x_after], axis=1)
    y_padded = jnp.concatenate([y_before, field, y_after], axis=2)
    z_padded = jnp.pad(field, ((0, 0), (0, 0), (0, 0), (2, 2)))
    total = second_diff(x_padded, 1, field.shape[1])
    total = total + second_diff(y_padded, 2, field.shape[2])
    total = total + second_diff(z_padded, 3, field.shape[3])
    return -0.5 * total + potential[None] * field


def shards(orbitals, potential, sign_bits, sampled_rows):
    chunks = lax.axis_size("xl")
    count = orbitals.shape[0]
    rows = orbitals.reshape((chunks, count // chunks) + orbitals.shape[1:])
    extra = jnp.broadcast_to(potential[None, None], (chunks, 1) + potential.shape)
    both = jnp.concatenate([rows, extra], axis=1).reshape((-1,) + orbitals.shape[1:])
    both = lax.all_to_all(both, "xl", 0, 1, tiled=True)
    spread, group_potential = both[: count // chunks], both[count // chunks]
    first = (apply_ham(spread, group_potential) - filter_center * spread) / filter_half
    second = 2.0 * (apply_ham(first, group_potential) - filter_center * first) / filter_half - spread
    spread_filtered = (
        2.0 * (apply_ham(second, group_potential) - filter_center * second) / filter_half - first
    )
    spread_applied = apply_ham(spread_filtered, group_potential)
    filtered = lax.all_to_all(spread_filtered, "xl", 1, 0, tiled=True)
    applied = lax.all_to_all(spread_applied, "xl", 1, 0, tiled=True)
    count = orbitals.shape[0]
    cells = orbitals.shape[1] * orbitals.shape[2] * orbitals.shape[3]
    stacked = jnp.concatenate([filtered, applied], axis=0)
    sign_block = (2 * sign_bits - 1).astype(jnp.float32)
    flat = (stacked * sign_block[None]).reshape(2 * count, -1, 128)
    mixed = jnp.einsum("nac,cd->adn", flat, hadamard_table(128), precision=HIGHEST)
    mixed = jnp.einsum("ba,adn->bdn", hadamard_table(cells // 128), mixed, precision=HIGHEST)
    mixed = mixed.reshape(cells, 2 * count)
    zh, xl, gy = (lax.axis_size(axis) for axis in BLOCK_AXES)
    order = sampled_rows[0, 0, :M].reshape(zh, xl, gy, -1).transpose(1, 0, 2, 3).reshape(-1)
    devices = zh * xl * gy
    picked = jnp.take(mixed, order, axis=0) / jnp.sqrt(jnp.float32(M * devices))
    y = lax.all_to_all(picked.reshape(xl, -1, 2 * count), "xl", 0, 0, tiled=True).sum(0)
    y = y.reshape(zh, gy, -1, 2 * count).transpose(1, 0, 2, 3)
    y = lax.all_to_all(y, "gy", 0, 0, tiled=True).sum(0)
    summed = exchange_sum(y, ("zh",)).transpose(2, 0, 1)
    share = lax.dynamic_index_in_dim(summed, lax.axis_index("zh"), 1, keepdims=False)
    share = share.reshape(2, count, -1)
    both = summed.reshape(2, count, -1)
    part_gram = jnp.dot(both[0], both[0].T, precision=HIGHEST)
    part_cross = jnp.dot(both[0], both[1].T, precision=HIGHEST)
    parts = exchange_sum(jnp.stack([part_gram, part_cross]), ("xl", "gy")) / cells
    gram, cross = parts[0], parts[1]
    lower = jnp.linalg.cholesky(gram)
    inverse = lax.linalg.triangular_solve(
        lower, jnp.eye(count, dtype=jnp.float32), left_side=True, lower=True
    )
    rotated = jnp.dot(inverse, filtered.reshape(count, -1), precision=HIGHEST).reshape(
        filtered.shape
    )
    inner = jnp.dot(jnp.dot(inverse, cross, precision=HIGHEST), inverse.T, precision=HIGHEST)
    projected = 0.5 * (inner + inner.T)
    return (rotated, share, projected)


def solution(mesh):
    groups = 4
    inner = Mesh(
        mesh.devices.reshape(groups, mesh.shape["gx"] // groups, mesh.shape["gy"]), ("zh", "xl", "gy")
    )
    gx = ("zh", "xl")
    in_specs = (
        P(None, gx, "gy", None),
        P(gx, "gy", None),
        P(gx, "gy", None),
        P(gx, "gy", None),
    )
    out_specs = (P(None, gx, "gy", None), P(None, None, gx + ("gy",)), P())
    return jax.shard_map(shards, mesh=inner, in_specs=in_specs, out_specs=out_specs, check_vma=False)
```

```python
import jax
import jax.numpy as jnp
from jax import lax
from jax.sharding import Mesh, PartitionSpec as P

M = 4096


HIGHEST = lax.Precision.HIGHEST
filter_center = 6.25
filter_half = 4.25


def halos(array, axis, dim, width):
    size, length = (lax.axis_size(axis), array.shape[dim])
    up = [(i, (i + 1) % size) for i in range(size - 1)]
    down = [(j, i) for i, j in up]
    last = lax.slice_in_dim(array, length - width, length, axis=dim)
    initial = lax.slice_in_dim(array, 0, width, axis=dim)
    before = lax.ppermute(last, axis, up)
    after = lax.ppermute(initial, axis, down)
    return before, after


BLOCK_AXES = ("zh", "xl", "gy")


def exchange_sum(x, axes):
    for axis in axes:
        size = lax.axis_size(axis)
        copies = jnp.broadcast_to(x[None], (size,) + x.shape)
        x = lax.all_to_all(copies, axis, 0, 0, tiled=True).sum(0)
    return x


def hadamard_table(order):
    index = jnp.arange(order, dtype=jnp.int32)
    parity = jnp.zeros((order, order), jnp.int32)
    for bit in range(order.bit_length() - 1):
        weight = 2**bit
        parity = parity + index[:, None] // weight % 2 * (index[None, :] // weight % 2)
    return (1 - 2 * (parity % 2)).astype(jnp.float32)


def second_diff(padded, axis, count):
    parts = [lax.slice_in_dim(padded, k, k + count, axis=axis) for k in range(5)]
    return (16.0 * (parts[1] + parts[3]) - (parts[0] + parts[4]) - 30.0 * parts[2]) / 12.0


def apply_ham(field, potential):
    x_before, x_after = halos(field, "zh", 1, 2)
    y_before, y_after = halos(field, "gy", 2, 2)
    x_padded = jnp.concatenate([x_before, field, x_after], axis=1)
    y_padded = jnp.concatenate([y_before, field, y_after], axis=2)
    z_padded = jnp.pad(field, ((0, 0), (0, 0), (0, 0), (2, 2)))
    total = second_diff(x_padded, 1, field.shape[1])
    total = total + second_diff(y_padded, 2, field.shape[2])
    total = total + second_diff(z_padded, 3, field.shape[3])
    return -0.5 * total + potential[None] * field


def shards(orbitals, potential, sign_bits, sampled_rows):
    chunks = lax.axis_size("xl")
    count = orbitals.shape[0]
    rows = orbitals.reshape((chunks, count // chunks) + orbitals.shape[1:])
    extra = jnp.broadcast_to(potential[None, None], (chunks, 1) + potential.shape)
    both = jnp.concatenate([rows, extra], axis=1).reshape((-1,) + orbitals.shape[1:])
    both = lax.all_to_all(both, "xl", 0, 1, tiled=True)
    spread, group_potential = both[: count // chunks], both[count // chunks]
    first = (apply_ham(spread, group_potential) - filter_center * spread) / filter_half
    second = 2.0 * (apply_ham(first, group_potential) - filter_center * first) / filter_half - spread
    spread_filtered = (
        2.0 * (apply_ham(second, group_potential) - filter_center * second) / filter_half - first
    )
    spread_applied = apply_ham(spread_filtered, group_potential)
    filtered = lax.all_to_all(spread_filtered, "xl", 1, 0, tiled=True)
    applied = lax.all_to_all(spread_applied, "xl", 1, 0, tiled=True)
    count = orbitals.shape[0]
    cells = orbitals.shape[1] * orbitals.shape[2] * orbitals.shape[3]
    sign_block = (2 * sign_bits - 1).astype(jnp.float32)

    def transform(field):
        flat = (field * sign_block[None]).reshape(count, -1, 128)
        mixed = jnp.einsum("nac,cd->adn", flat, hadamard_table(128), precision=HIGHEST)
        mixed = jnp.einsum("ba,adn->bdn", hadamard_table(cells // 128), mixed, precision=HIGHEST)
        return mixed.reshape(cells, count)

    mixed = jnp.concatenate([transform(filtered), transform(applied)], axis=1)
    zh, xl, gy = (lax.axis_size(axis) for axis in BLOCK_AXES)
    order = sampled_rows[0, 0, :M].reshape(zh, xl, gy, -1).transpose(1, 0, 2, 3).reshape(-1)
    devices = zh * xl * gy
    picked = jnp.take(mixed, order, axis=0) / jnp.sqrt(jnp.float32(M * devices))
    y = lax.all_to_all(picked.reshape(xl, -1, 2 * count), "xl", 0, 0, tiled=True).sum(0)
    y = y.reshape(zh, gy, -1, 2 * count).transpose(1, 0, 2, 3)
    y = lax.all_to_all(y, "gy", 0, 0, tiled=True).sum(0)
    summed = exchange_sum(y, ("zh",)).transpose(2, 0, 1)
    share = lax.dynamic_index_in_dim(summed, lax.axis_index("zh"), 1, keepdims=False)
    share = share.reshape(2, count, -1)
    both = summed.reshape(2, count, -1)
    part_gram = jnp.dot(both[0], both[0].T, precision=HIGHEST)
    part_cross = jnp.dot(both[0], both[1].T, precision=HIGHEST)
    parts = exchange_sum(jnp.stack([part_gram, part_cross]), ("xl", "gy")) / cells
    gram, cross = parts[0], parts[1]
    lower = jnp.linalg.cholesky(gram)
    inverse = lax.linalg.triangular_solve(
        lower, jnp.eye(count, dtype=jnp.float32), left_side=True, lower=True
    )
    rotated = jnp.dot(inverse, filtered.reshape(count, -1), precision=HIGHEST).reshape(
        filtered.shape
    )
    inner = jnp.dot(jnp.dot(inverse, cross, precision=HIGHEST), inverse.T, precision=HIGHEST)
    projected = 0.5 * (inner + inner.T)
    return (rotated, share, projected)


def solution(mesh):
    groups = 4
    inner = Mesh(
        mesh.devices.reshape(groups, mesh.shape["gx"] // groups, mesh.shape["gy"]), ("zh", "xl", "gy")
    )
    gx = ("zh", "xl")
    in_specs = (
        P(None, gx, "gy", None),
        P(gx, "gy", None),
        P(gx, "gy", None),
        P(gx, "gy", None),
    )
    out_specs = (P(None, gx, "gy", None), P(None, None, gx + ("gy",)), P())
    return jax.shard_map(shards, mesh=inner, in_specs=in_specs, out_specs=out_specs, check_vma=False)
```
